256 devices in a mesh: blk: 8 (over x, y_hi), batch: 32 (over y_lo, z, core).
Axes of the slice: x: 4, y: 4 (y_hi: 2, y_lo: 2; y = y_hi * 2 + y_lo), z: 8, core: 2. Of those that a mesh axis runs over, the one named last changes fastest.
Arguments:
- frame_one: bfloat16 [32, 4096, 128], P('batch', 'blk'), may hold values from -40 to 40
- frame_two: bfloat16 [32, 4096, 128], P('batch', 'blk'), may hold values from -40 to 40
- encoder_weight: bfloat16 [128, 256], replicated, may hold values from -0.5 to 0.5
- flow_grad: float32 [32, 2, 4096], P('batch', None, 'blk'), may hold values from -6 to 6
Outputs:
- flow: float32 [32, 2, 4096], P('batch', None, 'blk')
- grad_w: float32 [128, 256], replicated
The draws below stay inside these ranges and needn't reach their ends.
All inputs are finite; a program needn't handle non-finite values.
Results may differ from the reference program's by a relative error of at most 0.01.
Values may be sent and summed in bfloat16 or wider, within the bound.
No kernel may reach another device: no remote copies, remote signals or barrier semaphores. Data moves between devices by JAX's collectives and lax.ppermute only.
A program may use at most 64 MiB of HBM per device.

```python
import jax
import jax.numpy as jnp
from jax import lax

C = 256
CIN = 128
WIDTH = 240
PIX_DEV = 512
PIXELS = 4096
PAIRS = 32
N_BLK = 8


def frame_pairs(key):
    base = jax.random.fold_in(key, 7)
    key_first, key_second = jax.random.split(base, 2)
    shape = (PAIRS, PIXELS, CIN)
    first = 1.5 * jax.random.truncated_normal(key_first, -6.0, 6.0, shape, jnp.float32)
    second = 1.5 * jax.random.truncated_normal(key_second, -6.0, 6.0, shape, jnp.float32)
    return (first, second)


def draw_frame_one(key, part):
    return frame_pairs(key)[0].astype(jnp.bfloat16)


def draw_frame_two(key, part):
    return frame_pairs(key)[1].astype(jnp.bfloat16)


def shard_levels(own_key, shape, cuts, least, largest):
    gain = 1.0
    for dim, shards_of in cuts:
        draws = jax.random.uniform(jax.random.fold_in(jax.random.fold_in(own_key, 6), dim), (shards_of,), jnp.float32, least / len(cuts), largest / len(cuts))
        gain = gain * jnp.repeat(jnp.exp(draws), shape[dim] // shards_of).reshape((-1,) + (1,) * (len(shape) - 1 - dim))
    return gain


def gaussian(key, shape, spread, reach, shards=(), kind=jnp.bfloat16):
    values = jax.random.normal(key, shape, jnp.float32) * spread
    if len(shards) > 0:
        values = shard_levels(key, shape, shards, -0.22, 0.18) * values
    return jnp.clip(values, min=-reach, max=reach).astype(kind)


def setup_inputs(seed: int = 0) -> dict:
    streams_of = jax.random.split(jax.random.key(seed), 5)
    frame_one = draw_frame_one(jax.random.fold_in(streams_of[4], 71), 0)
    frame_two = draw_frame_two(jax.random.fold_in(streams_of[4], 71), 0)
    encoder_weight = gaussian(streams_of[2], (CIN, C), CIN ** -0.5, 0.5)
    flow_grad = gaussian(streams_of[3], (PAIRS, 2, PIXELS), 1.0, 6.0, ((0, 32), (2, 8)), jnp.float32)
    return dict(frame_one=frame_one, frame_two=frame_two, encoder_weight=encoder_weight, flow_grad=flow_grad)


def grid_coords(start, count):
    position = start + jnp.arange(count, dtype=jnp.int32)
    col_coord = (position % WIDTH).astype(jnp.float32) / 64.0
    row_coord = (position // WIDTH).astype(jnp.float32) / 8.0
    return col_coord, row_coord


def reference(frame_one, frame_two, encoder_weight, flow_grad):
    scaling = C ** -0.5

    def one_pair(operands):
        first_in, second_in, cotangent = operands
        first_feat = jnp.dot(first_in, encoder_weight, preferred_element_type=jnp.float32).astype(jnp.bfloat16)
        second_feat = jnp.dot(second_in, encoder_weight, preferred_element_type=jnp.float32).astype(jnp.bfloat16)
        key_col, key_row = grid_coords(0, PIXELS)

        def block_step(carry, block_index):
            key_accum, weight_accum = carry
            start = (block_index * PIX_DEV).astype(jnp.int32)
            query_feat = lax.dynamic_slice_in_dim(first_feat, start, PIX_DEV, 0)
            query_in = lax.dynamic_slice_in_dim(first_in, start, PIX_DEV, 0)
            grad_col = lax.dynamic_slice_in_dim(cotangent[0], start, PIX_DEV, 0)
            grad_row = lax.dynamic_slice_in_dim(cotangent[1], start, PIX_DEV, 0)
            own_col, own_row = grid_coords(start, PIX_DEV)
            logits = scaling * jnp.dot(query_feat, second_feat.T, preferred_element_type=jnp.float32)
            top = jnp.max(logits, axis=1, keepdims=True)
            expo = jnp.exp(logits - top)
            total = jnp.sum(expo, axis=1, keepdims=True)
            probs = expo / total
            mean_col = jnp.sum(probs * key_col[None, :], axis=1)
            mean_row = jnp.sum(probs * key_row[None, :], axis=1)
            inner = grad_col * mean_col + grad_row * mean_row
            slope = (probs * (grad_col[:, None] * key_col[None, :] + grad_row[:, None] * key_row[None, :] - inner[:, None])).astype(jnp.bfloat16)
            delta_one = (scaling * jnp.dot(slope, second_feat, preferred_element_type=jnp.float32)).astype(jnp.bfloat16)
            key_term = scaling * jnp.dot(slope.T, query_feat, preferred_element_type=jnp.float32)
            weight_accum = weight_accum + jnp.dot(query_in.T, delta_one, preferred_element_type=jnp.float32)
            block_flow = jnp.stack([mean_col - own_col, mean_row - own_row])
            return (key_accum + key_term, weight_accum), block_flow

        init = (jnp.zeros((PIXELS, C), jnp.float32), jnp.zeros((CIN, C), jnp.float32))
        (key_accum, weight_accum), flows = lax.scan(block_step, init, jnp.arange(N_BLK, dtype=jnp.int32))
        weight_accum = weight_accum + jnp.dot(second_in.astype(jnp.float32).T, key_accum, precision=lax.Precision.HIGHEST, preferred_element_type=jnp.float32)
        pair_flow = jnp.transpose(flows, (1, 0, 2)).reshape(2, PIXELS)
        return pair_flow, weight_accum

    flow, grads = lax.map(one_pair, (frame_one, frame_two, flow_grad))
    return flow, jnp.sum(grads, axis=0)
```

```python
import jax
import jax.numpy as jnp
from jax import lax
from jax.sharding import PartitionSpec as P

WIDTH = 240


def coords_of(position):
    col_coord = (position % WIDTH).astype(jnp.float32) / 64.0
    row_coord = (position // WIDTH).astype(jnp.float32) / 8.0
    return (col_coord, row_coord)


def butterfly_sum(x, axis, n):
    k = 1
    while k < n:
        x = x + lax.ppermute(x, axis, [(i, i ^ k) for i in range(n)])
        k *= 2
    return x


def body(frame_one, frame_two, encoder_weight, flow_grad, n_blk, n_batch):
    first_in = frame_one[0]
    second_in = frame_two[0]
    grad_col = flow_grad[0, 0]
    grad_row = flow_grad[0, 1]
    query_count = first_in.shape[0]
    channels = encoder_weight.shape[1]
    scaling = channels ** (-0.5)
    blk = lax.axis_index("blk")

    parts = [second_in] + [
        lax.ppermute(second_in, "blk", [(i, (i + k) % n_blk) for i in range(n_blk)])
        for k in range(1, n_blk)
    ]
    key_in = jnp.concatenate(parts, axis=0)
    source = (blk - jnp.arange(n_blk, dtype=jnp.int32)) % n_blk
    key_pos = (source[:, None] * query_count + jnp.arange(query_count, dtype=jnp.int32)[None, :]).reshape(-1)
    key_col, key_row = coords_of(key_pos)
    own_col, own_row = coords_of(blk * query_count + jnp.arange(query_count, dtype=jnp.int32))

    first_feat = jnp.dot(first_in, encoder_weight, preferred_element_type=jnp.float32).astype(jnp.bfloat16)
    key_feat = jnp.dot(key_in, encoder_weight, preferred_element_type=jnp.float32).astype(jnp.bfloat16)

    logits = scaling * jnp.dot(first_feat, key_feat.T, preferred_element_type=jnp.float32)
    top = jnp.max(logits, axis=1, keepdims=True)
    expo = jnp.exp(logits - top)
    total = jnp.sum(expo, axis=1, keepdims=True)
    probs = expo / total
    mean_col = jnp.sum(probs * key_col[None, :], axis=1)
    mean_row = jnp.sum(probs * key_row[None, :], axis=1)
    flow = jnp.stack([mean_col - own_col, mean_row - own_row])[None]

    inner = grad_col * mean_col + grad_row * mean_row
    slope = (
        probs * (grad_col[:, None] * key_col[None, :] + grad_row[:, None] * key_row[None, :] - inner[:, None])
    ).astype(jnp.bfloat16)
    delta_one = (scaling * jnp.dot(slope, key_feat, preferred_element_type=jnp.float32)).astype(jnp.bfloat16)
    key_term = scaling * jnp.dot(slope.T, first_feat, preferred_element_type=jnp.float32)
    local_grad = jnp.dot(first_in.T, delta_one, preferred_element_type=jnp.float32)
    local_grad = local_grad + jnp.dot(
        key_in.astype(jnp.float32).T,
        key_term,
        precision=lax.Precision.HIGHEST,
        preferred_element_type=jnp.float32,
    )
    grad_w = butterfly_sum(butterfly_sum(local_grad, "blk", n_blk), "batch", n_batch)
    return (flow, grad_w)


def solution(mesh):
    placed = (P("batch", "blk", None), P("batch", "blk", None), P(), P("batch", None, "blk"))
    n_blk = mesh.shape["blk"]
    n_batch = mesh.shape["batch"]

    def step(frame_one, frame_two, encoder_weight, flow_grad):
        return body(frame_one, frame_two, encoder_weight, flow_grad, n_blk, n_batch)

    return jax.shard_map(
        step, mesh=mesh, in_specs=placed, out_specs=(P("batch", None, "blk"), P()), check_vma=False
    )
```

```python
import jax
import jax.numpy as jnp
from jax import lax
from jax.sharding import PartitionSpec as P

WIDTH = 240


def coords_of(position):
    col_coord = (position % WIDTH).astype(jnp.float32) / 64.0
    row_coord = (position // WIDTH).astype(jnp.float32) / 8.0
    return (col_coord, row_coord)


def all_sum(x, axes, n):
    chunks = x.reshape(n, -1)
    mine = lax.all_to_all(chunks, axes, 0, 0, tiled=True).sum(axis=0)
    spread = jnp.broadcast_to(mine[None], chunks.shape)
    return lax.all_to_all(spread, axes, 0, 0, tiled=True).reshape(x.shape)


def body(frame_one, frame_two, encoder_weight, flow_grad, n_blk, n_batch):
    first_in = frame_one[0]
    second_in = frame_two[0]
    grad_col = flow_grad[0, 0]
    grad_row = flow_grad[0, 1]
    query_count = first_in.shape[0]
    channels = encoder_weight.shape[1]
    scaling = channels ** (-0.5)
    blk = lax.axis_index("blk")

    spread = jnp.broadcast_to(second_in[None], (n_blk,) + second_in.shape)
    key_in = lax.all_to_all(spread, "blk", 0, 0, tiled=True).reshape(-1, second_in.shape[1])
    key_col, key_row = coords_of(jnp.arange(key_in.shape[0], dtype=jnp.int32))
    own_col, own_row = coords_of(blk * query_count + jnp.arange(query_count, dtype=jnp.int32))

    first_feat = jnp.dot(first_in, encoder_weight, preferred_element_type=jnp.float32).astype(jnp.bfloat16)
    key_feat = jnp.dot(key_in, encoder_weight, preferred_element_type=jnp.float32).astype(jnp.bfloat16)

    logits = scaling * jnp.dot(first_feat, key_feat.T, preferred_element_type=jnp.float32)
    top = jnp.max(logits, axis=1, keepdims=True)
    expo = jnp.exp(logits - top)
    total = jnp.sum(expo, axis=1, keepdims=True)
    probs = expo / total
    mean_col = jnp.sum(probs * key_col[None, :], axis=1)
    mean_row = jnp.sum(probs * key_row[None, :], axis=1)
    flow = jnp.stack([mean_col - own_col, mean_row - own_row])[None]

    inner = grad_col * mean_col + grad_row * mean_row
    slope = (
        probs * (grad_col[:, None] * key_col[None, :] + grad_row[:, None] * key_row[None, :] - inner[:, None])
    ).astype(jnp.bfloat16)
    both = jnp.dot(slope, jnp.concatenate([key_feat, key_in], axis=1), preferred_element_type=jnp.float32)
    delta_one = (scaling * both[:, :channels]).astype(jnp.bfloat16)
    local_grad = jnp.dot(first_in.T, delta_one, preferred_element_type=jnp.float32)
    local_grad = local_grad + scaling * jnp.dot(
        both[:, channels:].T,
        first_feat.astype(jnp.float32),
        precision=lax.Precision.HIGHEST,
        preferred_element_type=jnp.float32,
    )
    grad_w = all_sum(local_grad, ("blk", "batch"), n_blk * n_batch)
    return (flow, grad_w)


def solution(mesh):
    placed = (P("batch", "blk", None), P("batch", "blk", None), P(), P("batch", None, "blk"))
    n_blk = mesh.shape["blk"]
    n_batch = mesh.shape["batch"]

    def step(frame_one, frame_two, encoder_weight, flow_grad):
        return body(frame_one, frame_two, encoder_weight, flow_grad, n_blk, n_batch)

    return jax.shard_map(
        step, mesh=mesh, in_specs=placed, out_specs=(P("batch", None, "blk"), P()), check_vma=False
    )
```

```python
import jax
import jax.numpy as jnp
from jax import lax
from jax.sharding import Mesh, PartitionSpec as P

WIDTH = 240


def coords_of(position):
    col_coord = (position % WIDTH).astype(jnp.float32) / 64.0
    row_coord = (position // WIDTH).astype(jnp.float32) / 8.0
    return (col_coord, row_coord)


def all_sum(x, axes, n):
    chunks = x.reshape(n, -1)
    mine = lax.all_to_all(chunks, axes, 0, 0, tiled=True).sum(axis=0)
    spread = jnp.broadcast_to(mine[None], chunks.shape)
    return lax.all_to_all(spread, axes, 0, 0, tiled=True).reshape(x.shape)


def body(frame_one, frame_two, encoder_weight, flow_grad, n_blk, n_batch):
    first_in = frame_one[0]
    second_in = frame_two[0]
    grad_col = flow_grad[0, 0]
    grad_row = flow_grad[0, 1]
    query_count = first_in.shape[0]
    channels = encoder_weight.shape[1]
    scaling = channels ** (-0.5)
    blk = lax.axis_index("blk")

    spread = jnp.broadcast_to(second_in[None], (n_blk,) + second_in.shape)
    key_in = lax.all_to_all(spread, "blk", 0, 0, tiled=True).reshape(-1, second_in.shape[1])
    key_col, key_row = coords_of(jnp.arange(key_in.shape[0], dtype=jnp.int32))
    own_col, own_row = coords_of(blk * query_count + jnp.arange(query_count, dtype=jnp.int32))

    first_feat = jnp.dot(first_in, encoder_weight, preferred_element_type=jnp.float32).astype(jnp.bfloat16)
    key_feat = jnp.dot(key_in, encoder_weight, preferred_element_type=jnp.float32).astype(jnp.bfloat16)

    logits = scaling * jnp.dot(first_feat, key_feat.T, preferred_element_type=jnp.float32)
    top = jnp.max(logits, axis=1, keepdims=True)
    expo = jnp.exp(logits - top)
    total = jnp.sum(expo, axis=1, keepdims=True)
    probs = expo / total
    mean_col = jnp.sum(probs * key_col[None, :], axis=1)
    mean_row = jnp.sum(probs * key_row[None, :], axis=1)
    flow = jnp.stack([mean_col - own_col, mean_row - own_row])[None]

    inner = grad_col * mean_col + grad_row * mean_row
    slope = (
        probs * (grad_col[:, None] * key_col[None, :] + grad_row[:, None] * key_row[None, :] - inner[:, None])
    ).astype(jnp.bfloat16)
    both = jnp.dot(slope, jnp.concatenate([key_feat, key_in], axis=1), preferred_element_type=jnp.float32)
    delta_one = (scaling * both[:, :channels]).astype(jnp.bfloat16)
    local_grad = jnp.dot(first_in.T, delta_one, preferred_element_type=jnp.float32)
    local_grad = local_grad + scaling * jnp.dot(
        both[:, channels:].T,
        first_feat.astype(jnp.float32),
        precision=lax.Precision.HIGHEST,
        preferred_element_type=jnp.float32,
    )
    local_grad = local_grad + lax.ppermute(local_grad, "core", [(0, 1), (1, 0)])
    grad_w = all_sum(local_grad, ("blk", "chip"), n_blk * n_batch // 2)
    return (flow, grad_w)


def solution(mesh):
    n_blk = mesh.shape["blk"]
    n_batch = mesh.shape["batch"]
    mesh = Mesh(mesh.devices.reshape(n_blk, n_batch // 2, 2), ("blk", "chip", "core"))
    batch = ("chip", "core")
    placed = (P(batch, "blk", None), P(batch, "blk", None), P(), P(batch, None, "blk"))

    def step(frame_one, frame_two, encoder_weight, flow_grad):
        return body(frame_one, frame_two, encoder_weight, flow_grad, n_blk, n_batch)

    return jax.shard_map(
        step, mesh=mesh, in_specs=placed, out_specs=(P(batch, None, "blk"), P()), check_vma=False
    )
```

```python
import functools

import jax
import jax.numpy as jnp
from jax import lax
from jax.experimental import pallas as pl
from jax.experimental.pallas import tpu as pltpu
from jax.sharding import Mesh, PartitionSpec as P

WIDTH = 240


def coords_of(position):
    col_coord = (position % WIDTH).astype(jnp.float32) / 64.0
    row_coord = (position // WIDTH).astype(jnp.float32) / 8.0
    return (col_coord, row_coord)


def all_sum(x, axes, n):
    chunks = x.reshape(n, -1)
    mine = lax.all_to_all(chunks, axes, 0, 0, tiled=True).sum(axis=0)
    spread = jnp.broadcast_to(mine[None], chunks.shape)
    return lax.all_to_all(spread, axes, 0, 0, tiled=True).reshape(x.shape)


def corr_kernel(ff_ref, kcat_ref, coord_ref, grad_ref, mean_ref, d1_ref, g2_ref, *, scaling, channels):
    ff = ff_ref[...]
    keys = kcat_ref[...]
    logits = scaling * lax.dot_general(
        ff, keys[:, :channels], (((1,), (1,)), ((), ())), preferred_element_type=jnp.float32
    )
    top = jnp.max(logits, axis=1, keepdims=True)
    expo = jnp.exp(logits - top)
    total = jnp.sum(expo, axis=1, keepdims=True)
    probs = expo / total
    key_col = coord_ref[0:1, :]
    key_row = coord_ref[1:2, :]
    mean_col = jnp.sum(probs * key_col, axis=1, keepdims=True)
    mean_row = jnp.sum(probs * key_row, axis=1, keepdims=True)
    grad_col = grad_ref[:, 0:1]
    grad_row = grad_ref[:, 1:2]
    inner = grad_col * mean_col + grad_row * mean_row
    slope = (probs * (grad_col * key_col + grad_row * key_row - inner)).astype(jnp.bfloat16)
    both = jnp.dot(slope, keys, preferred_element_type=jnp.float32)
    mean_ref[...] = jnp.concatenate([mean_col, mean_row], axis=1)
    d1_ref[...] = (scaling * both[:, :channels]).astype(jnp.bfloat16)
    g2_ref[...] = both[:, channels:]


def corr_call(first_feat, key_cat, coords, grads, scaling, channels, tile=128):
    rows = first_feat.shape[0]
    keys, width = key_cat.shape
    extra = width - channels
    kernel = functools.partial(corr_kernel, scaling=scaling, channels=channels)
    return pl.pallas_call(
        kernel,
        grid=(rows // tile,),
        in_specs=[
            pl.BlockSpec((tile, channels), lambda i: (i, 0)),
            pl.BlockSpec((keys, width), lambda i: (0, 0)),
            pl.BlockSpec(coords.shape, lambda i: (0, 0)),
            pl.BlockSpec((tile, grads.shape[1]), lambda i: (i, 0)),
        ],
        out_specs=[
            pl.BlockSpec((tile, 2), lambda i: (i, 0)),
            pl.BlockSpec((tile, channels), lambda i: (i, 0)),
            pl.BlockSpec((tile, extra), lambda i: (i, 0)),
        ],
        out_shape=[
            jax.ShapeDtypeStruct((rows, 2), jnp.float32),
            jax.ShapeDtypeStruct((rows, channels), jnp.bfloat16),
            jax.ShapeDtypeStruct((rows, extra), jnp.float32),
        ],
        compiler_params=pltpu.CompilerParams(vmem_limit_bytes=48 * 1024 * 1024),
    )(first_feat, key_cat, coords, grads)


def body(frame_one, frame_two, encoder_weight, flow_grad, n_blk, n_batch):
    first_in = frame_one[0]
    second_in = frame_two[0]
    grad_col = flow_grad[0, 0]
    grad_row = flow_grad[0, 1]
    query_count = first_in.shape[0]
    channels = encoder_weight.shape[1]
    scaling = channels ** (-0.5)
    blk = lax.axis_index("blk")

    spread = jnp.broadcast_to(second_in[None], (n_blk,) + second_in.shape)
    key_in = lax.all_to_all(spread, "blk", 0, 0, tiled=True).reshape(-1, second_in.shape[1])
    key_col, key_row = coords_of(jnp.arange(key_in.shape[0], dtype=jnp.int32))
    own_col, own_row = coords_of(blk * query_count + jnp.arange(query_count, dtype=jnp.int32))

    first_feat = jnp.dot(first_in, encoder_weight, preferred_element_type=jnp.float32).astype(jnp.bfloat16)
    key_feat = jnp.dot(key_in, encoder_weight, preferred_element_type=jnp.float32).astype(jnp.bfloat16)

    key_cat = jnp.concatenate([key_feat, key_in], axis=1)
    coords = jnp.stack([key_col, key_row])
    grads = jnp.stack([grad_col, grad_row], axis=1)
    means, delta_one, slope_two = corr_call(first_feat, key_cat, coords, grads, scaling, channels)
    flow = jnp.stack([means[:, 0] - own_col, means[:, 1] - own_row])[None]
    local_grad = jnp.dot(first_in.T, delta_one, preferred_element_type=jnp.float32)
    local_grad = local_grad + scaling * jnp.dot(
        slope_two.T,
        first_feat.astype(jnp.float32),
        precision=lax.Precision.HIGHEST,
        preferred_element_type=jnp.float32,
    )
    local_grad = local_grad + lax.ppermute(local_grad, "core", [(0, 1), (1, 0)])
    grad_w = all_sum(local_grad, ("blk", "chip"), n_blk * n_batch // 2)
    return (flow, grad_w)


def solution(mesh):
    n_blk = mesh.shape["blk"]
    n_batch = mesh.shape["batch"]
    mesh = Mesh(mesh.devices.reshape(n_blk, n_batch // 2, 2), ("blk", "chip", "core"))
    batch = ("chip", "core")
    placed = (P(batch, "blk", None), P(batch, "blk", None), P(), P(batch, None, "blk"))

    def step(frame_one, frame_two, encoder_weight, flow_grad):
        return body(frame_one, frame_two, encoder_weight, flow_grad, n_blk, n_batch)

    return jax.shard_map(
        step, mesh=mesh, in_specs=placed, out_specs=(P(batch, None, "blk"), P()), check_vma=False
    )
```

```python
import functools
import math

import jax
import jax.numpy as jnp
from jax import lax
from jax.experimental import pallas as pl
from jax.experimental.pallas import tpu as pltpu
from jax.sharding import Mesh, PartitionSpec as P

WIDTH = 240


def coords_of(position):
    col_coord = (position % WIDTH).astype(jnp.float32) / 64.0
    row_coord = (position // WIDTH).astype(jnp.float32) / 8.0
    return (col_coord, row_coord)


def all_sum(x, axes, n):
    chunks = x.reshape(n, -1)
    mine = lax.all_to_all(chunks, axes, 0, 0, tiled=True).sum(axis=0)
    spread = jnp.broadcast_to(mine[None], chunks.shape)
    return lax.all_to_all(spread, axes, 0, 0, tiled=True).reshape(x.shape)


def corr_kernel(ff_ref, kcat_ref, coord_ref, grad_ref, mean_ref, d1_ref, g2_ref, *, scaling, channels):
    keys = kcat_ref[...]
    logits = lax.dot_general(
        ff_ref[...], keys[:, :channels], (((1,), (1,)), ((), ())), preferred_element_type=jnp.float32
    )
    top = jnp.max(logits, axis=1, keepdims=True)
    expo = jnp.exp(logits - top)
    inv_total = 1.0 / jnp.sum(expo, axis=1, keepdims=True)
    key_col = coord_ref[0:1, :]
    key_row = coord_ref[1:2, :]
    mean_col = jnp.sum(expo * key_col, axis=1, keepdims=True) * inv_total
    mean_row = jnp.sum(expo * key_row, axis=1, keepdims=True) * inv_total
    grad_col = grad_ref[:, 0:1]
    grad_row = grad_ref[:, 1:2]
    inner = grad_col * mean_col + grad_row * mean_row
    slope = (expo * ((grad_col * inv_total) * key_col + (grad_row * inv_total) * key_row - inner * inv_total)).astype(
        jnp.bfloat16
    )
    both = jnp.dot(slope, keys, preferred_element_type=jnp.float32)
    mean_ref[...] = jnp.concatenate([mean_col, mean_row], axis=1)
    d1_ref[...] = (scaling * both[:, :channels]).astype(jnp.bfloat16)
    g2_ref[...] = both[:, channels:]


def corr_call(first_feat, key_cat, coords, grads, scaling, channels, tile=128):
    assert scaling == 2.0 ** round(math.log2(scaling))
    rows = first_feat.shape[0]
    keys, width = key_cat.shape
    extra = width - channels
    kernel = functools.partial(corr_kernel, scaling=scaling, channels=channels)
    return pl.pallas_call(
        kernel,
        grid=(rows // tile,),
        in_specs=[
            pl.BlockSpec((tile, channels), lambda i: (i, 0)),
            pl.BlockSpec((keys, width), lambda i: (0, 0)),
            pl.BlockSpec(coords.shape, lambda i: (0, 0)),
            pl.BlockSpec((tile, grads.shape[1]), lambda i: (i, 0)),
        ],
        out_specs=[
            pl.BlockSpec((tile, 2), lambda i: (i, 0)),
            pl.BlockSpec((tile, channels), lambda i: (i, 0)),
            pl.BlockSpec((tile, extra), lambda i: (i, 0)),
        ],
        out_shape=[
            jax.ShapeDtypeStruct((rows, 2), jnp.float32),
            jax.ShapeDtypeStruct((rows, channels), jnp.bfloat16),
            jax.ShapeDtypeStruct((rows, extra), jnp.float32),
        ],
        compiler_params=pltpu.CompilerParams(vmem_limit_bytes=48 * 1024 * 1024),
    )(first_feat * jnp.asarray(scaling, first_feat.dtype), key_cat, coords, grads)


def body(frame_one, frame_two, encoder_weight, flow_grad, n_blk, n_batch):
    first_in = frame_one[0]
    second_in = frame_two[0]
    grad_col = flow_grad[0, 0]
    grad_row = flow_grad[0, 1]
    query_count = first_in.shape[0]
    channels = encoder_weight.shape[1]
    scaling = channels ** (-0.5)
    blk = lax.axis_index("blk")

    spread = jnp.broadcast_to(second_in[None], (n_blk,) + second_in.shape)
    key_in = lax.all_to_all(spread, "blk", 0, 0, tiled=True).reshape(-1, second_in.shape[1])
    key_col, key_row = coords_of(jnp.arange(key_in.shape[0], dtype=jnp.int32))
    own_col, own_row = coords_of(blk * query_count + jnp.arange(query_count, dtype=jnp.int32))

    first_feat = jnp.dot(first_in, encoder_weight, preferred_element_type=jnp.float32).astype(jnp.bfloat16)
    key_feat = jnp.dot(key_in, encoder_weight, preferred_element_type=jnp.float32).astype(jnp.bfloat16)

    key_cat = jnp.concatenate([key_feat, key_in], axis=1)
    coords = jnp.stack([key_col, key_row])
    grads = jnp.stack([grad_col, grad_row], axis=1)
    means, delta_one, slope_two = corr_call(first_feat, key_cat, coords, grads, scaling, channels)
    flow = jnp.stack([means[:, 0] - own_col, means[:, 1] - own_row])[None]
    local_grad = jnp.dot(first_in.T, delta_one, preferred_element_type=jnp.float32)
    local_grad = local_grad + scaling * jnp.dot(
        slope_two.T,
        first_feat.astype(jnp.float32),
        precision=lax.Precision.HIGHEST,
        preferred_element_type=jnp.float32,
    )
    local_grad = local_grad + lax.ppermute(local_grad, "core", [(0, 1), (1, 0)])
    grad_w = all_sum(local_grad, ("blk", "chip"), n_blk * n_batch // 2)
    return (flow, grad_w)


def solution(mesh):
    n_blk = mesh.shape["blk"]
    n_batch = mesh.shape["batch"]
    mesh = Mesh(mesh.devices.reshape(n_blk, n_batch // 2, 2), ("blk", "chip", "core"))
    batch = ("chip", "core")
    placed = (P(batch, "blk", None), P(batch, "blk", None), P(), P(batch, None, "blk"))

    def step(frame_one, frame_two, encoder_weight, flow_grad):
        return body(frame_one, frame_two, encoder_weight, flow_grad, n_blk, n_batch)

    return jax.shard_map(
        step, mesh=mesh, in_specs=placed, out_specs=(P(batch, None, "blk"), P()), check_vma=False
    )
```

```python
import functools
import math

import jax
import jax.numpy as jnp
from jax import lax
from jax.experimental import pallas as pl
from jax.experimental.pallas import tpu as pltpu
from jax.sharding import Mesh, PartitionSpec as P

WIDTH = 240


def coords_of(position):
    col_coord = (position % WIDTH).astype(jnp.float32) / 64.0
    row_coord = (position // WIDTH).astype(jnp.float32) / 8.0
    return (col_coord, row_coord)


def all_sum(x, axes, n):
    chunks = x.reshape(n, -1)
    mine = lax.all_to_all(chunks, axes, 0, 0, tiled=True).sum(axis=0)
    spread = jnp.broadcast_to(mine[None], chunks.shape)
    return lax.all_to_all(spread, axes, 0, 0, tiled=True).reshape(x.shape)


def stats_kernel(ff_ref, kcat_ref, coord_ref, stat_ref, *, channels):
    logits = lax.dot_general(
        ff_ref[...], kcat_ref[:, :channels], (((1,), (1,)), ((), ())), preferred_element_type=jnp.float32
    )
    top = jnp.max(logits, axis=1, keepdims=True)
    expo = jnp.exp(logits - top)
    total = jnp.sum(expo, axis=1, keepdims=True)
    sum_col = jnp.sum(expo * coord_ref[0:1, :], axis=1, keepdims=True)
    sum_row = jnp.sum(expo * coord_ref[1:2, :], axis=1, keepdims=True)
    stat_ref[...] = jnp.concatenate([top, total, sum_col, sum_row], axis=1)


def slope_kernel(ff_ref, kcat_ref, coord_ref, coef_ref, both_ref, *, channels):
    keys = kcat_ref[...]
    logits = lax.dot_general(
        ff_ref[...], keys[:, :channels], (((1,), (1,)), ((), ())), preferred_element_type=jnp.float32
    )
    top = coef_ref[:, 0:1]
    factor = coef_ref[:, 1:2] * coord_ref[0:1, :] + coef_ref[:, 2:3] * coord_ref[1:2, :] + coef_ref[:, 3:4]
    slope = (jnp.exp(logits - top) * factor).astype(jnp.bfloat16)
    both_ref[...] = jnp.dot(slope, keys, preferred_element_type=jnp.float32)


def row_call(kernel, ff, kcat, coords, rows_in, out_width, channels, tile=128):
    rows = ff.shape[0]
    keys, width = kcat.shape
    in_specs = [
        pl.BlockSpec((tile, ff.shape[1]), lambda i: (i, 0)),
        pl.BlockSpec((keys, width), lambda i: (0, 0)),
        pl.BlockSpec(coords.shape, lambda i: (0, 0)),
    ]
    operands = [ff, kcat, coords]
    if rows_in is not None:
        in_specs.append(pl.BlockSpec((tile, rows_in.shape[1]), lambda i: (i, 0)))
        operands.append(rows_in)
    return pl.pallas_call(
        functools.partial(kernel, channels=channels),
        grid=(rows // tile,),
        in_specs=in_specs,
        out_specs=pl.BlockSpec((tile, out_width), lambda i: (i, 0)),
        out_shape=jax.ShapeDtypeStruct((rows, out_width), jnp.float32),
        compiler_params=pltpu.CompilerParams(vmem_limit_bytes=48 * 1024 * 1024),
    )(*operands)


def body(frame_one, frame_two, encoder_weight, flow_grad, n_x, n_yh, n_group):
    own_in = frame_one[0]
    second_in = frame_two[0]
    own_grad = flow_grad[0]
    count = own_in.shape[0]
    channels = encoder_weight.shape[1]
    scaling = channels ** (-0.5)
    assert scaling == 2.0 ** round(math.log2(scaling))
    xi = lax.axis_index("x")
    hi = lax.axis_index("yh")
    swap = [(0, 1), (1, 0)]

    spread = jnp.broadcast_to(second_in[None], (n_x,) + second_in.shape)
    key_in = lax.all_to_all(spread, "x", 0, 0, tiled=True).reshape(-1, second_in.shape[1])
    key_blk = jnp.arange(n_x, dtype=jnp.int32) * n_yh + hi
    key_pos = (key_blk[:, None] * count + jnp.arange(count, dtype=jnp.int32)[None, :]).reshape(-1)
    key_col, key_row = coords_of(key_pos)
    coords = jnp.stack([key_col, key_row])

    other_in = lax.ppermute(own_in, "yh", swap)
    other_grad = lax.ppermute(own_grad, "yh", swap)
    query_in = jnp.concatenate([own_in, other_in], axis=0)
    query_grad = jnp.concatenate([own_grad, other_grad], axis=1)

    query_feat = jnp.dot(query_in, encoder_weight, preferred_element_type=jnp.float32).astype(jnp.bfloat16)
    key_feat = jnp.dot(key_in, encoder_weight, preferred_element_type=jnp.float32).astype(jnp.bfloat16)
    key_cat = jnp.concatenate([key_feat, key_in], axis=1)
    scaled_feat = query_feat * jnp.asarray(scaling, query_feat.dtype)

    part = row_call(stats_kernel, scaled_feat, key_cat, coords, None, 4, channels)
    recv = lax.ppermute(part, "yh", swap)
    other = jnp.concatenate([recv[count:], recv[:count]], axis=0)
    top = jnp.maximum(part[:, 0], other[:, 0])
    w_mine = jnp.exp(part[:, 0] - top)
    w_other = jnp.exp(other[:, 0] - top)
    total = part[:, 1] * w_mine + other[:, 1] * w_other
    inv_total = 1.0 / total
    mean_col = (part[:, 2] * w_mine + other[:, 2] * w_other) * inv_total
    mean_row = (part[:, 3] * w_mine + other[:, 3] * w_other) * inv_total

    own_col, own_row = coords_of((xi * n_yh + hi) * count + jnp.arange(count, dtype=jnp.int32))
    flow = jnp.stack([mean_col[:count] - own_col, mean_row[:count] - own_row])[None]

    grad_col = query_grad[0]
    grad_row = query_grad[1]
    inner = grad_col * mean_col + grad_row * mean_row
    coef = jnp.stack([top, grad_col * inv_total, grad_row * inv_total, -inner * inv_total], axis=1)
    both = row_call(slope_kernel, scaled_feat, key_cat, coords, coef, key_cat.shape[1], channels)
    delta_one = scaling * both[:, :channels]
    local_grad = jnp.dot(
        query_in.astype(jnp.float32).T, delta_one, precision=lax.Precision.HIGHEST, preferred_element_type=jnp.float32
    )
    local_grad = local_grad + scaling * jnp.dot(
        both[:, channels:].T,
        query_feat.astype(jnp.float32),
        precision=lax.Precision.HIGHEST,
        preferred_element_type=jnp.float32,
    )
    local_grad = local_grad + lax.ppermute(local_grad, "core", swap)
    grad_w = all_sum(local_grad, ("x", "yh", "chip"), n_group)
    return (flow, grad_w)


def solution(mesh):
    n_blk = mesh.shape["blk"]
    n_batch = mesh.shape["batch"]
    n_yh = 2
    n_x = n_blk // n_yh
    mesh = Mesh(mesh.devices.reshape(n_x, n_yh, n_batch // 2, 2), ("x", "yh", "chip", "core"))
    blk = ("x", "yh")
    batch = ("chip", "core")
    placed = (P(batch, blk, None), P(batch, blk, None), P(), P(batch, None, blk))

    def step(frame_one, frame_two, encoder_weight, flow_grad):
        return body(frame_one, frame_two, encoder_weight, flow_grad, n_x, n_yh, n_x * n_yh * n_batch // 2)

    return jax.shard_map(
        step, mesh=mesh, in_specs=placed, out_specs=(P(batch, None, blk), P()), check_vma=False
    )
```

```python
import functools
import math

import jax
import jax.numpy as jnp
from jax import lax
from jax.experimental import pallas as pl
from jax.experimental.pallas import tpu as pltpu
from jax.sharding import Mesh, PartitionSpec as P

WIDTH = 240


def coords_of(position):
    col_coord = (position % WIDTH).astype(jnp.float32) / 64.0
    row_coord = (position // WIDTH).astype(jnp.float32) / 8.0
    return (col_coord, row_coord)


def all_sum(x, axes, n):
    chunks = x.reshape(n, -1)
    mine = lax.all_to_all(chunks, axes, 0, 0, tiled=True).sum(axis=0)
    spread = jnp.broadcast_to(mine[None], chunks.shape)
    return lax.all_to_all(spread, axes, 0, 0, tiled=True).reshape(x.shape)


def corr_kernel(ff_ref, kcat_ref, coord_ref, grad_ref, mean_ref, d1_ref, g2_ref, *, scaling, channels):
    keys = kcat_ref[...]
    logits = lax.dot_general(
        ff_ref[...], keys[:, :channels], (((1,), (1,)), ((), ())), preferred_element_type=jnp.float32
    )
    top = jnp.max(logits, axis=1, keepdims=True)
    expo = jnp.exp(logits - top)
    inv_total = 1.0 / jnp.sum(expo, axis=1, keepdims=True)
    key_col = coord_ref[0:1, :]
    key_row = coord_ref[1:2, :]
    mean_col = jnp.sum(expo * key_col, axis=1, keepdims=True) * inv_total
    mean_row = jnp.sum(expo * key_row, axis=1, keepdims=True) * inv_total
    grad_col = grad_ref[:, 0:1]
    grad_row = grad_ref[:, 1:2]
    inner = grad_col * mean_col + grad_row * mean_row
    slope = (expo * ((grad_col * inv_total) * key_col + (grad_row * inv_total) * key_row - inner * inv_total)).astype(
        jnp.bfloat16
    )
    both = jnp.dot(slope, keys, preferred_element_type=jnp.float32)
    mean_ref[...] = jnp.concatenate([mean_col, mean_row], axis=1)
    d1_ref[...] = (scaling * both[:, :channels]).astype(jnp.bfloat16)
    g2_ref[...] = both[:, channels:]


def corr_call(first_feat, key_cat, coords, grads, scaling, channels, tile=512):
    assert scaling == 2.0 ** round(math.log2(scaling))
    rows = first_feat.shape[0]
    tile = min(tile, rows)
    keys, width = key_cat.shape
    extra = width - channels
    kernel = functools.partial(corr_kernel, scaling=scaling, channels=channels)
    return pl.pallas_call(
        kernel,
        grid=(rows // tile,),
        in_specs=[
            pl.BlockSpec((tile, channels), lambda i: (i, 0)),
            pl.BlockSpec((keys, width), lambda i: (0, 0)),
            pl.BlockSpec(coords.shape, lambda i: (0, 0)),
            pl.BlockSpec((tile, grads.shape[1]), lambda i: (i, 0)),
        ],
        out_specs=[
            pl.BlockSpec((tile, 2), lambda i: (i, 0)),
            pl.BlockSpec((tile, channels), lambda i: (i, 0)),
            pl.BlockSpec((tile, extra), lambda i: (i, 0)),
        ],
        out_shape=[
            jax.ShapeDtypeStruct((rows, 2), jnp.float32),
            jax.ShapeDtypeStruct((rows, channels), jnp.bfloat16),
            jax.ShapeDtypeStruct((rows, extra), jnp.float32),
        ],
        compiler_params=pltpu.CompilerParams(vmem_limit_bytes=48 * 1024 * 1024),
    )(first_feat * jnp.asarray(scaling, first_feat.dtype), key_cat, coords, grads)


def body(frame_one, frame_two, encoder_weight, flow_grad, n_blk, n_batch):
    first_in = frame_one[0]
    second_in = frame_two[0]
    grad_col = flow_grad[0, 0]
    grad_row = flow_grad[0, 1]
    query_count = first_in.shape[0]
    channels = encoder_weight.shape[1]
    scaling = channels ** (-0.5)
    blk = lax.axis_index("blk")

    spread = jnp.broadcast_to(second_in[None], (n_blk,) + second_in.shape)
    key_in = lax.all_to_all(spread, "blk", 0, 0, tiled=True).reshape(-1, second_in.shape[1])
    key_col, key_row = coords_of(jnp.arange(key_in.shape[0], dtype=jnp.int32))
    own_col, own_row = coords_of(blk * query_count + jnp.arange(query_count, dtype=jnp.int32))

    first_feat = jnp.dot(first_in, encoder_weight, preferred_element_type=jnp.float32).astype(jnp.bfloat16)
    key_feat = jnp.dot(key_in, encoder_weight, preferred_element_type=jnp.float32).astype(jnp.bfloat16)

    key_cat = jnp.concatenate([key_feat, key_in], axis=1)
    coords = jnp.stack([key_col, key_row])
    grads = jnp.stack([grad_col, grad_row], axis=1)
    means, delta_one, slope_two = corr_call(first_feat, key_cat, coords, grads, scaling, channels)
    flow = jnp.stack([means[:, 0] - own_col, means[:, 1] - own_row])[None]
    local_grad = jnp.dot(first_in.T, delta_one, preferred_element_type=jnp.float32)
    local_grad = local_grad + scaling * jnp.dot(
        slope_two.T,
        first_feat.astype(jnp.float32),
        precision=lax.Precision.HIGHEST,
        preferred_element_type=jnp.float32,
    )
    local_grad = local_grad + lax.ppermute(local_grad, "core", [(0, 1), (1, 0)])
    grad_w = all_sum(local_grad, ("blk", "chip"), n_blk * n_batch // 2)
    return (flow, grad_w)


def solution(mesh):
    n_blk = mesh.shape["blk"]
    n_batch = mesh.shape["batch"]
    mesh = Mesh(mesh.devices.reshape(n_blk, n_batch // 2, 2), ("blk", "chip", "core"))
    batch = ("chip", "core")
    placed = (P(batch, "blk", None), P(batch, "blk", None), P(), P(batch, None, "blk"))

    def step(frame_one, frame_two, encoder_weight, flow_grad):
        return body(frame_one, frame_two, encoder_weight, flow_grad, n_blk, n_batch)

    return jax.shard_map(
        step, mesh=mesh, in_specs=placed, out_specs=(P(batch, None, "blk"), P()), check_vma=False
    )
```

```python
import functools
import math

import jax
import jax.numpy as jnp
from jax import lax
from jax.experimental import pallas as pl
from jax.experimental.pallas import tpu as pltpu
from jax.sharding import Mesh, PartitionSpec as P

WIDTH = 240


def coords_of(position):
    col_coord = (position % WIDTH).astype(jnp.float32) / 64.0
    row_coord = (position // WIDTH).astype(jnp.float32) / 8.0
    return (col_coord, row_coord)


def all_sum(x, axes, n):
    chunks = x.reshape(n, -1)
    mine = lax.all_to_all(chunks, axes, 0, 0, tiled=True).sum(axis=0)
    spread = jnp.broadcast_to(mine[None], chunks.shape)
    return lax.all_to_all(spread, axes, 0, 0, tiled=True).reshape(x.shape)


def corr_kernel(ff_ref, kin_ref, w_ref, coord_ref, grad_ref, mean_ref, d1_ref, g2_ref, *, scaling):
    key_in = kin_ref[...]
    key_feat = jnp.dot(key_in, w_ref[...], preferred_element_type=jnp.float32).astype(jnp.bfloat16)
    logits = lax.dot_general(ff_ref[...], key_feat, (((1,), (1,)), ((), ())), preferred_element_type=jnp.float32)
    top = jnp.max(logits, axis=1, keepdims=True)
    expo = jnp.exp(logits - top)
    inv_total = 1.0 / jnp.sum(expo, axis=1, keepdims=True)
    key_col = coord_ref[0:1, :]
    key_row = coord_ref[1:2, :]
    mean_col = jnp.sum(expo * key_col, axis=1, keepdims=True) * inv_total
    mean_row = jnp.sum(expo * key_row, axis=1, keepdims=True) * inv_total
    grad_col = grad_ref[:, 0:1]
    grad_row = grad_ref[:, 1:2]
    inner = grad_col * mean_col + grad_row * mean_row
    slope = (expo * ((grad_col * inv_total) * key_col + (grad_row * inv_total) * key_row - inner * inv_total)).astype(
        jnp.bfloat16
    )
    mean_ref[...] = jnp.concatenate([mean_col, mean_row], axis=1)
    d1_ref[...] = (scaling * jnp.dot(slope, key_feat, preferred_element_type=jnp.float32)).astype(jnp.bfloat16)
    g2_ref[...] = jnp.dot(slope, key_in, preferred_element_type=jnp.float32)


def corr_call(first_feat, key_in, weight, coords, grads, scaling, tile=512):
    assert scaling == 2.0 ** round(math.log2(scaling))
    rows, channels = first_feat.shape
    tile = min(tile, rows)
    keys, width = key_in.shape
    kernel = functools.partial(corr_kernel, scaling=scaling)
    return pl.pallas_call(
        kernel,
        grid=(rows // tile,),
        in_specs=[
            pl.BlockSpec((tile, channels), lambda i: (i, 0)),
            pl.BlockSpec((keys, width), lambda i: (0, 0)),
            pl.BlockSpec(weight.shape, lambda i: (0, 0)),
            pl.BlockSpec(coords.shape, lambda i: (0, 0)),
            pl.BlockSpec((tile, grads.shape[1]), lambda i: (i, 0)),
        ],
        out_specs=[
            pl.BlockSpec((tile, 2), lambda i: (i, 0)),
            pl.BlockSpec((tile, channels), lambda i: (i, 0)),
            pl.BlockSpec((tile, width), lambda i: (i, 0)),
        ],
        out_shape=[
            jax.ShapeDtypeStruct((rows, 2), jnp.float32),
            jax.ShapeDtypeStruct((rows, channels), jnp.bfloat16),
            jax.ShapeDtypeStruct((rows, width), jnp.float32),
        ],
        compiler_params=pltpu.CompilerParams(vmem_limit_bytes=48 * 1024 * 1024),
    )(first_feat * jnp.asarray(scaling, first_feat.dtype), key_in, weight, coords, grads)


def body(frame_one, frame_two, encoder_weight, flow_grad, n_blk, n_batch):
    first_in = frame_one[0]
    second_in = frame_two[0]
    grad_col = flow_grad[0, 0]
    grad_row = flow_grad[0, 1]
    query_count = first_in.shape[0]
    channels = encoder_weight.shape[1]
    scaling = channels ** (-0.5)
    blk = lax.axis_index("blk")

    spread = jnp.broadcast_to(second_in[None], (n_blk,) + second_in.shape)
    key_in = lax.all_to_all(spread, "blk", 0, 0, tiled=True).reshape(-1, second_in.shape[1])
    key_col, key_row = coords_of(jnp.arange(key_in.shape[0], dtype=jnp.int32))
    own_col, own_row = coords_of(blk * query_count + jnp.arange(query_count, dtype=jnp.int32))

    first_feat = jnp.dot(first_in, encoder_weight, preferred_element_type=jnp.float32).astype(jnp.bfloat16)

    coords = jnp.stack([key_col, key_row])
    grads = jnp.stack([grad_col, grad_row], axis=1)
    means, delta_one, slope_two = corr_call(first_feat, key_in, encoder_weight, coords, grads, scaling)
    flow = jnp.stack([means[:, 0] - own_col, means[:, 1] - own_row])[None]
    local_grad = jnp.dot(first_in.T, delta_one, preferred_element_type=jnp.float32)
    local_grad = local_grad + scaling * jnp.dot(
        slope_two.T,
        first_feat.astype(jnp.float32),
        precision=lax.Precision.HIGHEST,
        preferred_element_type=jnp.float32,
    )
    local_grad = local_grad + lax.ppermute(local_grad, "core", [(0, 1), (1, 0)])
    grad_w = all_sum(local_grad, ("blk", "chip"), n_blk * n_batch // 2)
    return (flow, grad_w)


def solution(mesh):
    n_blk = mesh.shape["blk"]
    n_batch = mesh.shape["batch"]
    mesh = Mesh(mesh.devices.reshape(n_blk, n_batch // 2, 2), ("blk", "chip", "core"))
    batch = ("chip", "core")
    placed = (P(batch, "blk", None), P(batch, "blk", None), P(), P(batch, None, "blk"))

    def step(frame_one, frame_two, encoder_weight, flow_grad):
        return body(frame_one, frame_two, encoder_weight, flow_grad, n_blk, n_batch)

    return jax.shard_map(
        step, mesh=mesh, in_specs=placed, out_specs=(P(batch, None, "blk"), P()), check_vma=False
    )
```

```python
import functools
import math

import jax
import jax.numpy as jnp
from jax import lax
from jax.experimental import pallas as pl
from jax.experimental.pallas import tpu as pltpu
from jax.sharding import Mesh, PartitionSpec as P

WIDTH = 240


def coords_of(position):
    col_coord = (position % WIDTH).astype(jnp.float32) / 64.0
    row_coord = (position // WIDTH).astype(jnp.float32) / 8.0
    return (col_coord, row_coord)


def all_sum(x, axes, n):
    chunks = x.reshape(n, -1)
    mine = lax.all_to_all(chunks, axes, 0, 0, tiled=True).sum(axis=0)
    spread = jnp.broadcast_to(mine[None], chunks.shape)
    return lax.all_to_all(spread, axes, 0, 0, tiled=True).reshape(x.shape)


def corr_kernel(ff_ref, qin_ref, kin_ref, w_ref, coord_ref, grad_ref, mean_ref, lg_ref, *, scaling):
    key_in = kin_ref[...]
    key_feat = jnp.dot(key_in, w_ref[...], preferred_element_type=jnp.float32).astype(jnp.bfloat16)
    logits = lax.dot_general(ff_ref[...], key_feat, (((1,), (1,)), ((), ())), preferred_element_type=jnp.float32)
    top = jnp.max(logits, axis=1, keepdims=True)
    expo = jnp.exp(logits - top)
    inv_total = 1.0 / jnp.sum(expo, axis=1, keepdims=True)
    key_col = coord_ref[0:1, :]
    key_row = coord_ref[1:2, :]
    mean_col = jnp.sum(expo * key_col, axis=1, keepdims=True) * inv_total
    mean_row = jnp.sum(expo * key_row, axis=1, keepdims=True) * inv_total
    grad_col = grad_ref[:, 0:1]
    grad_row = grad_ref[:, 1:2]
    inner = grad_col * mean_col + grad_row * mean_row
    slope = (expo * ((grad_col * inv_total) * key_col + (grad_row * inv_total) * key_row - inner * inv_total)).astype(
        jnp.bfloat16
    )
    mean_ref[...] = jnp.concatenate([mean_col, mean_row], axis=1)
    delta_one = (scaling * jnp.dot(slope, key_feat, preferred_element_type=jnp.float32)).astype(jnp.bfloat16)
    slope_two = jnp.dot(slope, key_in, preferred_element_type=jnp.float32)
    two_hi = slope_two.astype(jnp.bfloat16)
    two_lo = (slope_two - two_hi.astype(jnp.float32)).astype(jnp.bfloat16)
    tn = (((0,), (0,)), ((), ()))
    ff = ff_ref[...]
    local = lax.dot_general(qin_ref[...], delta_one, tn, preferred_element_type=jnp.float32)
    local = local + lax.dot_general(two_hi, ff, tn, preferred_element_type=jnp.float32)
    lg_ref[...] = local + lax.dot_general(two_lo, ff, tn, preferred_element_type=jnp.float32)


def corr_call(first_feat, first_in, key_in, weight, coords, grads, scaling):
    assert scaling == 2.0 ** round(math.log2(scaling))
    rows, channels = first_feat.shape
    width = key_in.shape[1]
    kernel = functools.partial(corr_kernel, scaling=scaling)
    whole = lambda a: pl.BlockSpec(a.shape, lambda i: (0,) * a.ndim)
    operands = (first_feat * jnp.asarray(scaling, first_feat.dtype), first_in, key_in, weight, coords, grads)
    return pl.pallas_call(
        kernel,
        grid=(1,),
        in_specs=[whole(a) for a in operands],
        out_specs=[pl.BlockSpec((rows, 2), lambda i: (0, 0)), pl.BlockSpec((width, channels), lambda i: (0, 0))],
        out_shape=[
            jax.ShapeDtypeStruct((rows, 2), jnp.float32),
            jax.ShapeDtypeStruct((width, channels), jnp.float32),
        ],
        compiler_params=pltpu.CompilerParams(vmem_limit_bytes=48 * 1024 * 1024),
    )(*operands)


def body(frame_one, frame_two, encoder_weight, flow_grad, n_blk, n_batch):
    first_in = frame_one[0]
    second_in = frame_two[0]
    grad_col = flow_grad[0, 0]
    grad_row = flow_grad[0, 1]
    query_count = first_in.shape[0]
    channels = encoder_weight.shape[1]
    scaling = channels ** (-0.5)
    blk = lax.axis_index("blk")

    spread = jnp.broadcast_to(second_in[None], (n_blk,) + second_in.shape)
    key_in = lax.all_to_all(spread, "blk", 0, 0, tiled=True).reshape(-1, second_in.shape[1])
    key_col, key_row = coords_of(jnp.arange(key_in.shape[0], dtype=jnp.int32))
    own_col, own_row = coords_of(blk * query_count + jnp.arange(query_count, dtype=jnp.int32))

    first_feat = jnp.dot(first_in, encoder_weight, preferred_element_type=jnp.float32).astype(jnp.bfloat16)

    coords = jnp.stack([key_col, key_row])
    grads = jnp.stack([grad_col, grad_row], axis=1)
    means, local_grad = corr_call(first_feat, first_in, key_in, encoder_weight, coords, grads, scaling)
    flow = jnp.stack([means[:, 0] - own_col, means[:, 1] - own_row])[None]
    local_grad = local_grad + lax.ppermute(local_grad, "core", [(0, 1), (1, 0)])
    grad_w = all_sum(local_grad, ("blk", "chip"), n_blk * n_batch // 2)
    return (flow, grad_w)


def solution(mesh):
    n_blk = mesh.shape["blk"]
    n_batch = mesh.shape["batch"]
    mesh = Mesh(mesh.devices.reshape(n_blk, n_batch // 2, 2), ("blk", "chip", "core"))
    batch = ("chip", "core")
    placed = (P(batch, "blk", None), P(batch, "blk", None), P(), P(batch, None, "blk"))

    def step(frame_one, frame_two, encoder_weight, flow_grad):
        return body(frame_one, frame_two, encoder_weight, flow_grad, n_blk, n_batch)

    return jax.shard_map(
        step, mesh=mesh, in_specs=placed, out_specs=(P(batch, None, "blk"), P()), check_vma=False
    )
```

```python
import functools
import math

import jax
import jax.numpy as jnp
from jax import lax
from jax.experimental import pallas as pl
from jax.experimental.pallas import tpu as pltpu
from jax.sharding import Mesh, PartitionSpec as P

WIDTH = 240


def coords_of(position):
    col_coord = (position % WIDTH).astype(jnp.float32) / 64.0
    row_coord = (position // WIDTH).astype(jnp.float32) / 8.0
    return (col_coord, row_coord)


def all_sum(x, axes, n):
    chunks = x.reshape(n, -1)
    mine = lax.all_to_all(chunks, axes, 0, 0, tiled=True).sum(axis=0)
    spread = jnp.broadcast_to(mine[None], chunks.shape)
    return lax.all_to_all(spread, axes, 0, 0, tiled=True).reshape(x.shape)


def copies_kernel(src_ref, out_ref):
    out_ref[...] = src_ref[...][None]


def copies(x, n):
    return pl.pallas_call(
        copies_kernel,
        grid=(n,),
        in_specs=[pl.BlockSpec(x.shape, lambda i: (0, 0))],
        out_specs=pl.BlockSpec((1,) + x.shape, lambda i: (i, 0, 0)),
        out_shape=jax.ShapeDtypeStruct((n,) + x.shape, x.dtype),
    )(x)


def corr_kernel(ff_ref, qin_ref, kin_ref, w_ref, coord_ref, grad_ref, mean_ref, lg_ref, *, scaling):
    key_in = kin_ref[...]
    key_feat = jnp.dot(key_in, w_ref[...], preferred_element_type=jnp.float32).astype(jnp.bfloat16)
    logits = lax.dot_general(ff_ref[...], key_feat, (((1,), (1,)), ((), ())), preferred_element_type=jnp.float32)
    top = jnp.max(logits, axis=1, keepdims=True)
    expo = jnp.exp(logits - top)
    inv_total = 1.0 / jnp.sum(expo, axis=1, keepdims=True)
    key_col = coord_ref[0:1, :]
    key_row = coord_ref[1:2, :]
    mean_col = jnp.sum(expo * key_col, axis=1, keepdims=True) * inv_total
    mean_row = jnp.sum(expo * key_row, axis=1, keepdims=True) * inv_total
    grad_col = grad_ref[:, 0:1]
    grad_row = grad_ref[:, 1:2]
    inner = grad_col * mean_col + grad_row * mean_row
    slope = (expo * ((grad_col * inv_total) * key_col + (grad_row * inv_total) * key_row - inner * inv_total)).astype(
        jnp.bfloat16
    )
    mean_ref[...] = jnp.concatenate([mean_col, mean_row], axis=1)
    delta_one = (scaling * jnp.dot(slope, key_feat, preferred_element_type=jnp.float32)).astype(jnp.bfloat16)
    slope_two = jnp.dot(slope, key_in, preferred_element_type=jnp.float32)
    two_hi = slope_two.astype(jnp.bfloat16)
    two_lo = (slope_two - two_hi.astype(jnp.float32)).astype(jnp.bfloat16)
    tn = (((0,), (0,)), ((), ()))
    ff = ff_ref[...]
    local = lax.dot_general(qin_ref[...], delta_one, tn, preferred_element_type=jnp.float32)
    local = local + lax.dot_general(two_hi, ff, tn, preferred_element_type=jnp.float32)
    lg_ref[...] = local + lax.dot_general(two_lo, ff, tn, preferred_element_type=jnp.float32)


def corr_call(first_feat, first_in, key_in, weight, coords, grads, scaling):
    assert scaling == 2.0 ** round(math.log2(scaling))
    rows, channels = first_feat.shape
    width = key_in.shape[1]
    kernel = functools.partial(corr_kernel, scaling=scaling)
    whole = lambda a: pl.BlockSpec(a.shape, lambda i: (0,) * a.ndim)
    operands = (first_feat * jnp.asarray(scaling, first_feat.dtype), first_in, key_in, weight, coords, grads)
    return pl.pallas_call(
        kernel,
        grid=(1,),
        in_specs=[whole(a) for a in operands],
        out_specs=[pl.BlockSpec((rows, 2), lambda i: (0, 0)), pl.BlockSpec((width, channels), lambda i: (0, 0))],
        out_shape=[
            jax.ShapeDtypeStruct((rows, 2), jnp.float32),
            jax.ShapeDtypeStruct((width, channels), jnp.float32),
        ],
        compiler_params=pltpu.CompilerParams(vmem_limit_bytes=48 * 1024 * 1024),
    )(*operands)


def body(frame_one, frame_two, encoder_weight, flow_grad, n_blk, n_batch):
    first_in = frame_one[0]
    second_in = frame_two[0]
    grad_col = flow_grad[0, 0]
    grad_row = flow_grad[0, 1]
    query_count = first_in.shape[0]
    channels = encoder_weight.shape[1]
    scaling = channels ** (-0.5)
    blk = lax.axis_index("blk")

    spread = copies(second_in, n_blk)
    key_in = lax.all_to_all(spread, "blk", 0, 0, tiled=True).reshape(-1, second_in.shape[1])
    key_col, key_row = coords_of(jnp.arange(key_in.shape[0], dtype=jnp.int32))
    own_col, own_row = coords_of(blk * query_count + jnp.arange(query_count, dtype=jnp.int32))

    first_feat = jnp.dot(first_in, encoder_weight, preferred_element_type=jnp.float32).astype(jnp.bfloat16)

    coords = jnp.stack([key_col, key_row])
    grads = jnp.stack([grad_col, grad_row], axis=1)
    means, local_grad = corr_call(first_feat, first_in, key_in, encoder_weight, coords, grads, scaling)
    flow = jnp.stack([means[:, 0] - own_col, means[:, 1] - own_row])[None]
    local_grad = local_grad + lax.ppermute(local_grad, "core", [(0, 1), (1, 0)])
    grad_w = all_sum(local_grad, ("blk", "chip"), n_blk * n_batch // 2)
    return (flow, grad_w)


def solution(mesh):
    n_blk = mesh.shape["blk"]
    n_batch = mesh.shape["batch"]
    mesh = Mesh(mesh.devices.reshape(n_blk, n_batch // 2, 2), ("blk", "chip", "core"))
    batch = ("chip", "core")
    placed = (P(batch, "blk", None), P(batch, "blk", None), P(), P(batch, None, "blk"))

    def step(frame_one, frame_two, encoder_weight, flow_grad):
        return body(frame_one, frame_two, encoder_weight, flow_grad, n_blk, n_batch)

    return jax.shard_map(
        step, mesh=mesh, in_specs=placed, out_specs=(P(batch, None, "blk"), P()), check_vma=False
    )
```

```python
import functools
import math

import jax
import jax.numpy as jnp
from jax import lax
from jax.experimental import pallas as pl
from jax.experimental.pallas import tpu as pltpu
from jax.sharding import Mesh, PartitionSpec as P

WIDTH = 240


def coords_of(position):
    col_coord = (position % WIDTH).astype(jnp.float32) / 64.0
    row_coord = (position // WIDTH).astype(jnp.float32) / 8.0
    return (col_coord, row_coord)


def all_sum(x, axes, n):
    chunks = x.reshape(n, -1)
    mine = lax.all_to_all(chunks, axes, 0, 0, tiled=True).sum(axis=0)
    spread = jnp.broadcast_to(mine[None], chunks.shape)
    return lax.all_to_all(spread, axes, 0, 0, tiled=True).reshape(x.shape)


def corr_kernel(ff_ref, qin_ref, kin_ref, w_ref, coord_ref, grad_ref, mean_ref, lg_ref, *, scaling):
    key_in = kin_ref[...]
    key_feat = jnp.dot(key_in, w_ref[...], preferred_element_type=jnp.float32).astype(jnp.bfloat16)
    logits = lax.dot_general(ff_ref[...], key_feat, (((1,), (1,)), ((), ())), preferred_element_type=jnp.float32)
    top = jnp.max(logits, axis=1, keepdims=True)
    expo = jnp.exp(logits - top)
    inv_total = 1.0 / jnp.sum(expo, axis=1, keepdims=True)
    key_col = coord_ref[0:1, :]
    key_row = coord_ref[1:2, :]
    mean_col = jnp.sum(expo * key_col, axis=1, keepdims=True) * inv_total
    mean_row = jnp.sum(expo * key_row, axis=1, keepdims=True) * inv_total
    grad_col = grad_ref[:, 0:1]
    grad_row = grad_ref[:, 1:2]
    inner = grad_col * mean_col + grad_row * mean_row
    slope = (expo * ((grad_col * inv_total) * key_col + (grad_row * inv_total) * key_row - inner * inv_total)).astype(
        jnp.bfloat16
    )
    mean_ref[...] = jnp.concatenate([mean_col, mean_row], axis=1)
    delta_one = (scaling * jnp.dot(slope, key_feat, preferred_element_type=jnp.float32)).astype(jnp.bfloat16)
    slope_two = jnp.dot(slope, key_in, preferred_element_type=jnp.float32)
    two_hi = slope_two.astype(jnp.bfloat16)
    two_lo = (slope_two - two_hi.astype(jnp.float32)).astype(jnp.bfloat16)
    tn = (((0,), (0,)), ((), ()))
    ff = ff_ref[...]
    local = lax.dot_general(qin_ref[...], delta_one, tn, preferred_element_type=jnp.float32)
    local = local + lax.dot_general(two_hi, ff, tn, preferred_element_type=jnp.float32)
    lg_ref[...] = local + lax.dot_general(two_lo, ff, tn, preferred_element_type=jnp.float32)


def corr_call(first_feat, first_in, key_in, weight, coords, grads, scaling):
    assert scaling == 2.0 ** round(math.log2(scaling))
    rows, channels = first_feat.shape
    width = key_in.shape[1]
    kernel = functools.partial(corr_kernel, scaling=scaling)
    whole = lambda a: pl.BlockSpec(a.shape, lambda i: (0,) * a.ndim)
    operands = (first_feat * jnp.asarray(scaling, first_feat.dtype), first_in, key_in, weight, coords, grads)
    return pl.pallas_call(
        kernel,
        grid=(1,),
        in_specs=[whole(a) for a in operands],
        out_specs=[pl.BlockSpec((rows, 2), lambda i: (0, 0)), pl.BlockSpec((width, channels), lambda i: (0, 0))],
        out_shape=[
            jax.ShapeDtypeStruct((rows, 2), jnp.float32),
            jax.ShapeDtypeStruct((width, channels), jnp.float32),
        ],
        compiler_params=pltpu.CompilerParams(vmem_limit_bytes=48 * 1024 * 1024),
    )(*operands)


def body(frame_one, frame_two, encoder_weight, flow_grad, n_blk, n_batch):
    first_in = frame_one[0]
    second_in = frame_two[0]
    grad_col = flow_grad[0, 0]
    grad_row = flow_grad[0, 1]
    query_count = first_in.shape[0]
    channels = encoder_weight.shape[1]
    scaling = channels ** (-0.5)
    blk = lax.axis_index("blk")

    spread = jnp.broadcast_to(second_in[None], (n_blk,) + second_in.shape)
    key_in = lax.all_to_all(spread, "blk", 0, 0, tiled=True).reshape(-1, second_in.shape[1])
    key_col, key_row = coords_of(jnp.arange(key_in.shape[0], dtype=jnp.int32))
    own_col, own_row = coords_of(blk * query_count + jnp.arange(query_count, dtype=jnp.int32))

    first_feat = jnp.dot(first_in, encoder_weight, preferred_element_type=jnp.float32).astype(jnp.bfloat16)

    coords = jnp.stack([key_col, key_row])
    grads = jnp.stack([grad_col, grad_row], axis=1)
    means, local_grad = corr_call(first_feat, first_in, key_in, encoder_weight, coords, grads, scaling)
    flow = jnp.stack([means[:, 0] - own_col, means[:, 1] - own_row])[None]
    grad_w = all_sum(local_grad, ("blk", "chip", "core"), n_blk * n_batch)
    return (flow, grad_w)


def solution(mesh):
    n_blk = mesh.shape["blk"]
    n_batch = mesh.shape["batch"]
    mesh = Mesh(mesh.devices.reshape(n_blk, n_batch // 2, 2), ("blk", "chip", "core"))
    batch = ("chip", "core")
    placed = (P(batch, "blk", None), P(batch, "blk", None), P(), P(batch, None, "blk"))

    def step(frame_one, frame_two, encoder_weight, flow_grad):
        return body(frame_one, frame_two, encoder_weight, flow_grad, n_blk, n_batch)

    return jax.shard_map(
        step, mesh=mesh, in_specs=placed, out_specs=(P(batch, None, "blk"), P()), check_vma=False
    )
```

```python
import functools
import math

import jax
import jax.numpy as jnp
from jax import lax
from jax.experimental import pallas as pl
from jax.experimental.pallas import tpu as pltpu
from jax.sharding import Mesh, PartitionSpec as P

WIDTH = 240


def coords_of(position):
    col_coord = (position % WIDTH).astype(jnp.float32) / 64.0
    row_coord = (position // WIDTH).astype(jnp.float32) / 8.0
    return (col_coord, row_coord)


def all_sum(x, axes, n):
    chunks = x.reshape(n, -1)
    mine = lax.all_to_all(chunks, axes, 0, 0, tiled=True).sum(axis=0)
    mine = mine + lax.ppermute(mine, "core", [(0, 1), (1, 0)])
    spread = jnp.broadcast_to(mine[None], chunks.shape)
    return lax.all_to_all(spread, axes, 0, 0, tiled=True).reshape(x.shape)


def corr_kernel(ff_ref, qin_ref, kin_ref, w_ref, coord_ref, grad_ref, mean_ref, lg_ref, *, scaling):
    key_in = kin_ref[...]
    key_feat = jnp.dot(key_in, w_ref[...], preferred_element_type=jnp.float32).astype(jnp.bfloat16)
    logits = lax.dot_general(ff_ref[...], key_feat, (((1,), (1,)), ((), ())), preferred_element_type=jnp.float32)
    top = jnp.max(logits, axis=1, keepdims=True)
    expo = jnp.exp(logits - top)
    inv_total = 1.0 / jnp.sum(expo, axis=1, keepdims=True)
    key_col = coord_ref[0:1, :]
    key_row = coord_ref[1:2, :]
    mean_col = jnp.sum(expo * key_col, axis=1, keepdims=True) * inv_total
    mean_row = jnp.sum(expo * key_row, axis=1, keepdims=True) * inv_total
    grad_col = grad_ref[:, 0:1]
    grad_row = grad_ref[:, 1:2]
    inner = grad_col * mean_col + grad_row * mean_row
    slope = (expo * ((grad_col * inv_total) * key_col + (grad_row * inv_total) * key_row - inner * inv_total)).astype(
        jnp.bfloat16
    )
    mean_ref[...] = jnp.concatenate([mean_col, mean_row], axis=1)
    delta_one = (scaling * jnp.dot(slope, key_feat, preferred_element_type=jnp.float32)).astype(jnp.bfloat16)
    slope_two = jnp.dot(slope, key_in, preferred_element_type=jnp.float32)
    two_hi = slope_two.astype(jnp.bfloat16)
    two_lo = (slope_two - two_hi.astype(jnp.float32)).astype(jnp.bfloat16)
    tn = (((0,), (0,)), ((), ()))
    ff = ff_ref[...]
    local = lax.dot_general(qin_ref[...], delta_one, tn, preferred_element_type=jnp.float32)
    local = local + lax.dot_general(two_hi, ff, tn, preferred_element_type=jnp.float32)
    lg_ref[...] = local + lax.dot_general(two_lo, ff, tn, preferred_element_type=jnp.float32)


def corr_call(first_feat, first_in, key_in, weight, coords, grads, scaling):
    assert scaling == 2.0 ** round(math.log2(scaling))
    rows, channels = first_feat.shape
    width = key_in.shape[1]
    kernel = functools.partial(corr_kernel, scaling=scaling)
    whole = lambda a: pl.BlockSpec(a.shape, lambda i: (0,) * a.ndim)
    operands = (first_feat * jnp.asarray(scaling, first_feat.dtype), first_in, key_in, weight, coords, grads)
    return pl.pallas_call(
        kernel,
        grid=(1,),
        in_specs=[whole(a) for a in operands],
        out_specs=[pl.BlockSpec((rows, 2), lambda i: (0, 0)), pl.BlockSpec((width, channels), lambda i: (0, 0))],
        out_shape=[
            jax.ShapeDtypeStruct((rows, 2), jnp.float32),
            jax.ShapeDtypeStruct((width, channels), jnp.float32),
        ],
        compiler_params=pltpu.CompilerParams(vmem_limit_bytes=48 * 1024 * 1024),
    )(*operands)


def body(frame_one, frame_two, encoder_weight, flow_grad, n_blk, n_batch):
    first_in = frame_one[0]
    second_in = frame_two[0]
    grad_col = flow_grad[0, 0]
    grad_row = flow_grad[0, 1]
    query_count = first_in.shape[0]
    channels = encoder_weight.shape[1]
    scaling = channels ** (-0.5)
    blk = lax.axis_index("blk")

    spread = jnp.broadcast_to(second_in[None], (n_blk,) + second_in.shape)
    key_in = lax.all_to_all(spread, "blk", 0, 0, tiled=True).reshape(-1, second_in.shape[1])
    key_col, key_row = coords_of(jnp.arange(key_in.shape[0], dtype=jnp.int32))
    own_col, own_row = coords_of(blk * query_count + jnp.arange(query_count, dtype=jnp.int32))

    first_feat = jnp.dot(first_in, encoder_weight, preferred_element_type=jnp.float32).astype(jnp.bfloat16)

    coords = jnp.stack([key_col, key_row])
    grads = jnp.stack([grad_col, grad_row], axis=1)
    means, local_grad = corr_call(first_feat, first_in, key_in, encoder_weight, coords, grads, scaling)
    flow = jnp.stack([means[:, 0] - own_col, means[:, 1] - own_row])[None]
    grad_w = all_sum(local_grad, ("blk", "chip"), n_blk * n_batch // 2)
    return (flow, grad_w)


def solution(mesh):
    n_blk = mesh.shape["blk"]
    n_batch = mesh.shape["batch"]
    mesh = Mesh(mesh.devices.reshape(n_blk, n_batch // 2, 2), ("blk", "chip", "core"))
    batch = ("chip", "core")
    placed = (P(batch, "blk", None), P(batch, "blk", None), P(), P(batch, None, "blk"))

    def step(frame_one, frame_two, encoder_weight, flow_grad):
        return body(frame_one, frame_two, encoder_weight, flow_grad, n_blk, n_batch)

    return jax.shard_map(
        step, mesh=mesh, in_specs=placed, out_specs=(P(batch, None, "blk"), P()), check_vma=False
    )
```
